512 devices in a mesh: grp: 16 (over z), dev: 32 (over y, x, core).
Axes of the slice: x: 4, y: 4, z: 16, core: 2. Of those that a mesh axis runs over, the one named last changes fastest.
Arguments:
- basis: float32 [2097152, 128], P(('grp', 'dev')), may hold values from -40 to 40
- raw: float32 [2097152, 64], P(('grp', 'dev')), may hold values from -200 to 200, as said below
- recur: float32 [128, 64], replicated, may hold values from -6 to 6
Outputs:
- lanczos: float32 [2097152, 64], P(('grp', 'dev'))
- factor: float32 [64, 64], replicated
- coeffs: float32 [128, 64], replicated
The draws below stay inside these ranges and needn't reach their ends.
Inputs may be any that keep to these rules, and one draw needn't show every extreme that they name: `raw`: finite real values.
All inputs are finite; a program needn't handle non-finite values.
Results may differ from the reference program's by a relative error of at most 0.0003.
Values sent between devices are 32-bit elements; how exact they have to be, the bound alone decides.
No kernel may reach another device: no remote copies, remote signals or barrier semaphores. Data moves between devices by JAX's collectives and lax.ppermute only.
A program may use at most 64 MiB of HBM per device.

```python
import jax
import jax.numpy as jnp
from jax import lax

BASIS = 128
K = 64
ROWS = 2097152


def draw_raw(key, part):
    k_base, k_rows, k_cols = jax.random.split(key, 3)
    position = jnp.arange(ROWS, dtype=jnp.float32) / ROWS
    row_scale = jnp.exp(jnp.log(3.0) * position + jax.random.uniform(k_rows, (ROWS,), minval=0.0, maxval=jnp.log(10.0)))
    col_scale = jnp.exp(jax.random.uniform(k_cols, (K,), minval=0.0, maxval=jnp.log(10.0)))
    base = jax.random.normal(k_base, (ROWS, K))
    values = base * row_scale[:, None] * col_scale[None, :] / 10.0
    return jnp.clip(values, -200.0, 200.0).astype(jnp.float32)


def cholesky_upper(moments):
    size = moments.shape[0]
    positions = jnp.arange(size)
    highest = lax.Precision.HIGHEST

    def column_step(column_index, lower_part):
        current = lax.dynamic_slice_in_dim(lower_part, column_index, 1, 0)[0]
        column_values = lax.dynamic_slice_in_dim(moments, column_index, 1, 1)[:, 0]
        reduced = column_values - jnp.dot(lower_part, current, precision=highest)
        pivot_value = jnp.sqrt(lax.dynamic_slice_in_dim(reduced, column_index, 1, 0)[0])
        fresh_column = jnp.where(positions > column_index, reduced / pivot_value, jnp.where(positions == column_index, pivot_value, jnp.zeros_like(reduced)))
        return jnp.where(positions[None, :] == column_index, fresh_column[:, None], lower_part)
    lower_part = lax.fori_loop(0, size, column_step, jnp.zeros_like(moments))
    return lower_part.T


def upper_inverse(upper):
    size = upper.shape[0]
    positions = jnp.arange(size)
    highest = lax.Precision.HIGHEST

    def row_step(count, result):
        row_index = size - 1 - count
        current = lax.dynamic_slice_in_dim(upper, row_index, 1, 0)[0]
        diagonal_value = lax.dynamic_slice_in_dim(current, row_index, 1, 0)[0]
        target = (positions == row_index).astype(upper.dtype)
        fresh_row = (target - jnp.dot(current, result, precision=highest)) / diagonal_value
        return jnp.where(positions[:, None] == row_index, fresh_row[None, :], result)
    return lax.fori_loop(0, size, row_step, jnp.zeros_like(upper))


def orthonormal_pass(matrix):
    highest = lax.Precision.HIGHEST
    gram = jnp.dot(matrix.T, matrix, precision=highest) / matrix.shape[0]
    gram = 0.5 * (gram + gram.T)
    upper = cholesky_upper(gram)
    inverse = upper_inverse(upper)
    return jnp.dot(matrix, inverse, precision=highest)


def draw_basis(key, part):
    base_key = jax.random.fold_in(key, 7341)
    k_base = jax.random.fold_in(base_key, 0)
    k_rows = jax.random.fold_in(base_key, 1)
    k_mix = jax.random.fold_in(base_key, 3)
    row_scale = jnp.exp(jax.random.uniform(k_rows, (ROWS,), minval=0.0, maxval=jnp.log(10.0)))
    base = jax.random.truncated_normal(k_base, -4.0, 4.0, (ROWS, BASIS))
    matrix = (base * row_scale[:, None]).astype(jnp.float32)
    matrix = orthonormal_pass(orthonormal_pass(matrix))
    mixing = 0.01 * jax.random.normal(k_mix, (BASIS, BASIS))
    mixing = jnp.triu(mixing, 1) + jnp.eye(BASIS, dtype=jnp.float32)
    values = jnp.dot(matrix, mixing.astype(jnp.float32), precision=lax.Precision.HIGHEST)
    return jnp.clip(values, -40.0, 40.0).astype(jnp.float32)


def scatter_about(rng, dims, deviation, most, held_as=jnp.bfloat16):
    return jnp.clip(deviation * jax.random.normal(rng, dims, jnp.float32), -most, most).astype(held_as)


def setup_inputs(seed: int = 0) -> dict:
    arg_keys = jax.random.split(jax.random.key(seed), 4)
    basis = draw_basis(jax.random.fold_in(arg_keys[3], 71), 0)
    raw = draw_raw(jax.random.fold_in(arg_keys[3], 71), 0)
    recur = scatter_about(arg_keys[2], (BASIS, K), 1.0, 6.0, jnp.float32)
    return dict(basis=basis, raw=raw, recur=recur)


def small_factor(moments):
    size = moments.shape[0]
    positions = jnp.arange(size)
    highest = lax.Precision.HIGHEST
    lower_part = jnp.zeros_like(moments)
    for column_index in range(size):
        reduced = moments[:, column_index] - jnp.dot(lower_part, lower_part[column_index], precision=highest)
        pivot_value = jnp.sqrt(reduced[column_index])
        fresh_column = jnp.where(positions > column_index, reduced / pivot_value, jnp.where(positions == column_index, pivot_value, jnp.zeros_like(reduced)))
        lower_part = jnp.where(positions[None, :] == column_index, fresh_column[:, None], lower_part)
    return lower_part.T

def small_inverse(upper):
    size = upper.shape[0]
    positions = jnp.arange(size)
    highest = lax.Precision.HIGHEST
    result = jnp.zeros_like(upper)
    for count in range(size):
        row_index = size - 1 - count
        current = upper[row_index]
        target = (positions == row_index).astype(upper.dtype)
        fresh_row = (target - jnp.dot(current, result, precision=highest)) / current[row_index]
        result = jnp.where(positions[:, None] == row_index, fresh_row[None, :], result)
    return result

def factor_pair(moments):
    size = moments.shape[0]
    if size <= 8:
        upper = small_factor(moments)
        return (upper, small_inverse(upper))
    highest = lax.Precision.HIGHEST
    half = size // 2
    upper_one, inverse_one = factor_pair(moments[:half, :half])
    corner = jnp.dot(inverse_one.T, moments[:half, half:], precision=highest)
    rest = moments[half:, half:] - jnp.dot(corner.T, corner, precision=highest)
    upper_two, inverse_two = factor_pair(rest)
    zeros_block = jnp.zeros((size - half, half), moments.dtype)
    upper = jnp.block([[upper_one, corner], [zeros_block, upper_two]])
    inverse_corner = -jnp.dot(inverse_one, jnp.dot(corner, inverse_two, precision=highest), precision=highest)
    inverse = jnp.block([[inverse_one, inverse_corner], [zeros_block, inverse_two]])
    return (upper, inverse)

def reference(basis, raw, recur):
    total = basis.shape[0]
    highest = lax.Precision.HIGHEST
    block = raw - jnp.dot(basis, recur, precision=highest)
    first = jnp.dot(basis.T, block, precision=highest) / total
    once = block - jnp.dot(basis, first, precision=highest)
    second = jnp.dot(basis.T, once, precision=highest) / total
    twice = once - jnp.dot(basis, second, precision=highest)
    gram = jnp.dot(twice.T, twice, precision=highest) / total
    gram = 0.5 * (gram + gram.T)
    factor, inverse = factor_pair(gram)
    lanczos = jnp.dot(twice, inverse, precision=highest)
    return (lanczos, factor, first + second)
```

```python
import jax
import jax.numpy as jnp
from jax import lax
from jax.sharding import Mesh
from jax.sharding import PartitionSpec as P
from jax.experimental import pallas as pl
from jax.experimental.pallas import tpu as pltpu

DEV = ("dev_0", "dev_1", "dev_2")
GRP_DEV = ("grp", "dev_0", "dev_1", "dev_2")


def filled_up(lines, devices):
    spare = -lines.shape[0] % devices
    if not spare:
        return lines
    return jnp.concatenate([lines, jnp.zeros((spare, *lines.shape[1:]), lines.dtype)])


def from_everyone(shard, axis):
    copies = jnp.broadcast_to(shard, (lax.axis_size(axis), *shard.shape))
    return lax.all_to_all(copies, axis, split_axis=0, concat_axis=0, tiled=True)


def laid_out(parts, dim):
    dims = list(parts.shape[1:])
    dims[dim] *= parts.shape[0]
    return jnp.moveaxis(parts, 0, dim).reshape(dims)


def gather_axes(shard, axes, dim):
    far, near = axes
    first = from_everyone(shard, far)
    parts = jnp.swapaxes(from_everyone(first, near), 0, 1)
    return laid_out(parts.reshape(-1, *shard.shape), dim)


def in_blocks(shard, dim, devices):
    before, after = (shard.shape[:dim], shard.shape[dim + 1 :])
    return jnp.moveaxis(shard.reshape(*before, devices, -1, *after), dim, 0)


def sum_at_owner(shard, axis, dim):
    devices = lax.axis_size(axis)
    parts = lax.all_to_all(in_blocks(shard, dim, devices), axis, 0, 0, tiled=True)
    return jnp.sum(parts, axis=0)


def sum_by_axis(shard, axes, dim):
    far, near = axes
    own = sum_at_owner(in_blocks(shard, dim, lax.axis_size(far)), near, dim + 1)
    return jnp.sum(lax.all_to_all(own, far, 0, 0, tiled=True), axis=0)


def nested_sum(shard, axes):
    padded = filled_up(shard, lax.axis_size(axes[0]) * lax.axis_size(axes[1]))
    whole = gather_axes(sum_by_axis(padded, axes, 0), axes, 0)
    return lax.slice_in_dim(whole, 0, len(shard)).reshape(shard.shape)


def packed_total(arrays, axis):
    vector, at, gathered = (jnp.concatenate([a.reshape(-1) for a in arrays]), 0, [])
    running = nested_sum(vector, axis)
    for a in arrays:
        gathered.append(running[at : at + a.size].reshape(a.shape))
        at += a.size
    return tuple(gathered)


def small_factor(moments):
    size = moments.shape[0]
    positions = jnp.arange(size)
    highest = lax.Precision.HIGHEST
    lower_part = jnp.zeros_like(moments)
    for column_index in range(size):
        reduced = moments[:, column_index] - jnp.dot(
            lower_part, lower_part[column_index], precision=highest
        )
        pivot_value = jnp.sqrt(reduced[column_index])
        fresh_column = jnp.where(
            positions > column_index,
            reduced / pivot_value,
            jnp.where(positions == column_index, pivot_value, jnp.zeros_like(reduced)),
        )
        lower_part = jnp.where(
            positions[None, :] == column_index, fresh_column[:, None], lower_part
        )
    return lower_part.T


def small_inverse(upper):
    size = upper.shape[0]
    positions = jnp.arange(size)
    highest = lax.Precision.HIGHEST
    result = jnp.zeros_like(upper)
    for count in range(size):
        row_index = size - 1 - count
        current = upper[row_index]
        target = (positions == row_index).astype(upper.dtype)
        fresh_row = (target - jnp.dot(current, result, precision=highest)) / current[row_index]
        result = jnp.where(positions[:, None] == row_index, fresh_row[None, :], result)
    return result


def factor_pair(moments):
    size = moments.shape[0]
    if size <= 8:
        upper = small_factor(moments)
        return (upper, small_inverse(upper))
    highest = lax.Precision.HIGHEST
    half = size // 2
    upper_one, inverse_one = factor_pair(moments[:half, :half])
    corner = jnp.dot(inverse_one.T, moments[:half, half:], precision=highest)
    rest = moments[half:, half:] - jnp.dot(corner.T, corner, precision=highest)
    upper_two, inverse_two = factor_pair(rest)
    zeros_block = jnp.zeros((size - half, half), moments.dtype)
    upper = jnp.block([[upper_one, corner], [zeros_block, upper_two]])
    inverse_corner = -jnp.dot(
        inverse_one, jnp.dot(corner, inverse_two, precision=highest), precision=highest
    )
    inverse = jnp.block([[inverse_one, inverse_corner], [zeros_block, inverse_two]])
    return (upper, inverse)


def eliminate(augmented_ref, factor_ref, inverse_t_ref):
    matrix = augmented_ref[...]
    size = matrix.shape[0]
    rows = lax.broadcasted_iota(jnp.int32, matrix.shape, 0)
    lanes = lax.broadcasted_iota(jnp.int32, matrix.shape, 1)
    row_ids = rows[:, :1]

    def step(index, matrix):
        pivot_row = jnp.sum(jnp.where(rows == index, matrix, 0.0), axis=0, keepdims=True)
        column = jnp.sum(jnp.where(lanes == index, matrix, 0.0), axis=1, keepdims=True)
        pivot = jnp.sum(jnp.where(lanes[:1] == index, pivot_row, 0.0), axis=1, keepdims=True)
        scale = jnp.where(row_ids > index, column / pivot, 0.0)
        return matrix - scale * pivot_row

    matrix = lax.fori_loop(0, size, step, matrix)
    diagonal = jnp.sum(jnp.where(lanes == rows, matrix, 0.0), axis=1, keepdims=True)
    root = jnp.sqrt(diagonal)
    scaled = matrix / root
    upper = jnp.where(lanes > rows, scaled, jnp.where(lanes == rows, root, 0.0))
    factor_ref[...] = upper[:, :size]
    inverse_t_ref[...] = scaled[:, size:]


def factor_and_inverse_t(gram):
    size = gram.shape[0]
    augmented = jnp.concatenate([gram, jnp.eye(size, dtype=gram.dtype)], axis=1)
    vmem = pl.BlockSpec(memory_space=pltpu.VMEM)
    return pl.pallas_call(
        eliminate,
        out_shape=(
            jax.ShapeDtypeStruct((size, size), gram.dtype),
            jax.ShapeDtypeStruct((size, size), gram.dtype),
        ),
        in_specs=[vmem],
        out_specs=(vmem, vmem),
    )(augmented)


def shards(basis, raw, recur):
    highest = lax.Precision.HIGHEST
    total = basis.shape[0] * lax.axis_size("grp") * lax.axis_size(DEV)
    block = raw - jnp.dot(basis, recur, precision=highest)
    cross, basis_gram, block_gram = packed_total(
        (
            jnp.dot(basis.T, block, precision=highest) / total,
            jnp.dot(basis.T, basis, precision=highest) / total,
            jnp.dot(block.T, block, precision=highest) / total,
        ),
        (("grp", "dev_0"), ("dev_1", "dev_2")),
    )
    second = cross - jnp.dot(basis_gram, cross, precision=highest)
    coeffs = cross + second
    twice = block - jnp.dot(basis, coeffs, precision=highest)
    mixed = jnp.dot(cross.T, coeffs, precision=highest)
    gram = (
        block_gram
        - mixed
        - mixed.T
        + jnp.dot(coeffs.T, jnp.dot(basis_gram, coeffs, precision=highest), precision=highest)
    )
    gram = 0.5 * (gram + gram.T)
    factor, inverse_t = factor_and_inverse_t(gram)
    lanczos = lax.dot_general(twice, inverse_t, (((1,), (1,)), ((), ())), precision=highest)
    return (lanczos, factor, coeffs)


def solution(mesh):
    torus = Mesh(
        mesh.devices.reshape(mesh.shape["grp"], 4, 4, 2), ("grp", "dev_0", "dev_1", "dev_2")
    )
    in_specs = (P(GRP_DEV, None), P(GRP_DEV, None), P())
    out_specs = (P(GRP_DEV, None), P(), P())
    return jax.shard_map(
        shards, mesh=torus, in_specs=in_specs, out_specs=out_specs, check_vma=False
    )
```

```python
import jax
import jax.numpy as jnp
from jax import lax
from jax.sharding import Mesh
from jax.sharding import PartitionSpec as P
from jax.experimental import pallas as pl
from jax.experimental.pallas import tpu as pltpu

DEV = ("dev_0", "dev_1", "dev_2")
GRP_DEV = ("grp", "dev_0", "dev_1", "dev_2")


def filled_up(lines, devices):
    spare = -lines.shape[0] % devices
    if not spare:
        return lines
    return jnp.concatenate([lines, jnp.zeros((spare, *lines.shape[1:]), lines.dtype)])


def from_everyone(shard, axis):
    copies = jnp.broadcast_to(shard, (lax.axis_size(axis), *shard.shape))
    return lax.all_to_all(copies, axis, split_axis=0, concat_axis=0, tiled=True)


def laid_out(parts, dim):
    dims = list(parts.shape[1:])
    dims[dim] *= parts.shape[0]
    return jnp.moveaxis(parts, 0, dim).reshape(dims)


def gather_axes(shard, axes, dim):
    far, near = axes
    first = from_everyone(shard, far)
    parts = jnp.swapaxes(from_everyone(first, near), 0, 1)
    return laid_out(parts.reshape(-1, *shard.shape), dim)


def in_blocks(shard, dim, devices):
    before, after = (shard.shape[:dim], shard.shape[dim + 1 :])
    return jnp.moveaxis(shard.reshape(*before, devices, -1, *after), dim, 0)


def sum_at_owner(shard, axis, dim):
    devices = lax.axis_size(axis)
    parts = lax.all_to_all(in_blocks(shard, dim, devices), axis, 0, 0, tiled=True)
    return jnp.sum(parts, axis=0)


def sum_by_axis(shard, axes, dim):
    far, near = axes
    own = sum_at_owner(in_blocks(shard, dim, lax.axis_size(far)), near, dim + 1)
    return jnp.sum(lax.all_to_all(own, far, 0, 0, tiled=True), axis=0)


def nested_sum(shard, axes):
    padded = filled_up(shard, lax.axis_size(axes[0]) * lax.axis_size(axes[1]))
    whole = gather_axes(sum_by_axis(padded, axes, 0), axes, 0)
    return lax.slice_in_dim(whole, 0, len(shard)).reshape(shard.shape)


def packed_total(arrays, axis):
    vector, at, gathered = (jnp.concatenate([a.reshape(-1) for a in arrays]), 0, [])
    running = lax.psum(vector, axis)
    for a in arrays:
        gathered.append(running[at : at + a.size].reshape(a.shape))
        at += a.size
    return tuple(gathered)


def small_factor(moments):
    size = moments.shape[0]
    positions = jnp.arange(size)
    highest = lax.Precision.HIGHEST
    lower_part = jnp.zeros_like(moments)
    for column_index in range(size):
        reduced = moments[:, column_index] - jnp.dot(
            lower_part, lower_part[column_index], precision=highest
        )
        pivot_value = jnp.sqrt(reduced[column_index])
        fresh_column = jnp.where(
            positions > column_index,
            reduced / pivot_value,
            jnp.where(positions == column_index, pivot_value, jnp.zeros_like(reduced)),
        )
        lower_part = jnp.where(
            positions[None, :] == column_index, fresh_column[:, None], lower_part
        )
    return lower_part.T


def small_inverse(upper):
    size = upper.shape[0]
    positions = jnp.arange(size)
    highest = lax.Precision.HIGHEST
    result = jnp.zeros_like(upper)
    for count in range(size):
        row_index = size - 1 - count
        current = upper[row_index]
        target = (positions == row_index).astype(upper.dtype)
        fresh_row = (target - jnp.dot(current, result, precision=highest)) / current[row_index]
        result = jnp.where(positions[:, None] == row_index, fresh_row[None, :], result)
    return result


def factor_pair(moments):
    size = moments.shape[0]
    if size <= 8:
        upper = small_factor(moments)
        return (upper, small_inverse(upper))
    highest = lax.Precision.HIGHEST
    half = size // 2
    upper_one, inverse_one = factor_pair(moments[:half, :half])
    corner = jnp.dot(inverse_one.T, moments[:half, half:], precision=highest)
    rest = moments[half:, half:] - jnp.dot(corner.T, corner, precision=highest)
    upper_two, inverse_two = factor_pair(rest)
    zeros_block = jnp.zeros((size - half, half), moments.dtype)
    upper = jnp.block([[upper_one, corner], [zeros_block, upper_two]])
    inverse_corner = -jnp.dot(
        inverse_one, jnp.dot(corner, inverse_two, precision=highest), precision=highest
    )
    inverse = jnp.block([[inverse_one, inverse_corner], [zeros_block, inverse_two]])
    return (upper, inverse)


def eliminate(augmented_ref, factor_ref, inverse_t_ref):
    matrix = augmented_ref[...]
    size = matrix.shape[0]
    rows = lax.broadcasted_iota(jnp.int32, matrix.shape, 0)
    lanes = lax.broadcasted_iota(jnp.int32, matrix.shape, 1)
    row_ids = rows[:, :1]

    def step(index, matrix):
        pivot_row = jnp.sum(jnp.where(rows == index, matrix, 0.0), axis=0, keepdims=True)
        column = jnp.sum(jnp.where(lanes == index, matrix, 0.0), axis=1, keepdims=True)
        pivot = jnp.sum(jnp.where(lanes[:1] == index, pivot_row, 0.0), axis=1, keepdims=True)
        scale = jnp.where(row_ids > index, column / pivot, 0.0)
        return matrix - scale * pivot_row

    matrix = lax.fori_loop(0, size, step, matrix)
    diagonal = jnp.sum(jnp.where(lanes == rows, matrix, 0.0), axis=1, keepdims=True)
    root = jnp.sqrt(diagonal)
    scaled = matrix / root
    upper = jnp.where(lanes > rows, scaled, jnp.where(lanes == rows, root, 0.0))
    factor_ref[...] = upper[:, :size]
    inverse_t_ref[...] = scaled[:, size:]


def factor_and_inverse_t(gram):
    size = gram.shape[0]
    augmented = jnp.concatenate([gram, jnp.eye(size, dtype=gram.dtype)], axis=1)
    vmem = pl.BlockSpec(memory_space=pltpu.VMEM)
    return pl.pallas_call(
        eliminate,
        out_shape=(
            jax.ShapeDtypeStruct((size, size), gram.dtype),
            jax.ShapeDtypeStruct((size, size), gram.dtype),
        ),
        in_specs=[vmem],
        out_specs=(vmem, vmem),
    )(augmented)


def shards(basis, raw, recur):
    highest = lax.Precision.HIGHEST
    total = basis.shape[0] * lax.axis_size("grp") * lax.axis_size(DEV)
    block = raw - jnp.dot(basis, recur, precision=highest)
    cross, basis_gram, block_gram = packed_total(
        (
            jnp.dot(basis.T, block, precision=highest) / total,
            jnp.dot(basis.T, basis, precision=highest) / total,
            jnp.dot(block.T, block, precision=highest) / total,
        ),
        GRP_DEV,
    )
    second = cross - jnp.dot(basis_gram, cross, precision=highest)
    coeffs = cross + second
    twice = block - jnp.dot(basis, coeffs, precision=highest)
    mixed = jnp.dot(cross.T, coeffs, precision=highest)
    gram = (
        block_gram
        - mixed
        - mixed.T
        + jnp.dot(coeffs.T, jnp.dot(basis_gram, coeffs, precision=highest), precision=highest)
    )
    gram = 0.5 * (gram + gram.T)
    factor, inverse_t = factor_and_inverse_t(gram)
    lanczos = lax.dot_general(twice, inverse_t, (((1,), (1,)), ((), ())), precision=highest)
    return (lanczos, factor, coeffs)


def solution(mesh):
    torus = Mesh(
        mesh.devices.reshape(mesh.shape["grp"], 4, 4, 2), ("grp", "dev_0", "dev_1", "dev_2")
    )
    in_specs = (P(GRP_DEV, None), P(GRP_DEV, None), P())
    out_specs = (P(GRP_DEV, None), P(), P())
    return jax.shard_map(
        shards, mesh=torus, in_specs=in_specs, out_specs=out_specs, check_vma=False
    )
```

```python
import jax
import jax.numpy as jnp
from jax import lax
from jax.sharding import Mesh
from jax.sharding import PartitionSpec as P
from jax.experimental import pallas as pl
from jax.experimental.pallas import tpu as pltpu

DEV = ("dev_0", "dev_1", "dev_2")
GRP_DEV = ("grp", "dev_0", "dev_1", "dev_2")


def group_size(axes):
    size = 1
    for axis in axes:
        size *= lax.axis_size(axis)
    return size


def from_everyone(shard, axes):
    copies = jnp.broadcast_to(shard, (group_size(axes), *shard.shape))
    return lax.all_to_all(copies, axes, 0, 0, tiled=True)


def scatter_sum(vector, axes):
    parts = lax.all_to_all(vector.reshape(group_size(axes), -1), axes, 0, 0, tiled=True)
    return jnp.sum(parts, axis=0)


def nested_sum(vector, axes):
    near, far = axes
    devices = group_size(near)
    padded = jnp.pad(vector, (0, -vector.shape[0] % devices))
    own = scatter_sum(padded, near)
    own = jnp.sum(from_everyone(own, far), axis=0)
    whole = from_everyone(own, near).reshape(-1)
    return whole[: vector.shape[0]]


def packed_total(arrays, axis):
    vector, at, gathered = (jnp.concatenate([a.reshape(-1) for a in arrays]), 0, [])
    running = nested_sum(vector, axis)
    for a in arrays:
        gathered.append(running[at : at + a.size].reshape(a.shape))
        at += a.size
    return tuple(gathered)


def small_factor(moments):
    size = moments.shape[0]
    positions = jnp.arange(size)
    highest = lax.Precision.HIGHEST
    lower_part = jnp.zeros_like(moments)
    for column_index in range(size):
        reduced = moments[:, column_index] - jnp.dot(
            lower_part, lower_part[column_index], precision=highest
        )
        pivot_value = jnp.sqrt(reduced[column_index])
        fresh_column = jnp.where(
            positions > column_index,
            reduced / pivot_value,
            jnp.where(positions == column_index, pivot_value, jnp.zeros_like(reduced)),
        )
        lower_part = jnp.where(
            positions[None, :] == column_index, fresh_column[:, None], lower_part
        )
    return lower_part.T


def small_inverse(upper):
    size = upper.shape[0]
    positions = jnp.arange(size)
    highest = lax.Precision.HIGHEST
    result = jnp.zeros_like(upper)
    for count in range(size):
        row_index = size - 1 - count
        current = upper[row_index]
        target = (positions == row_index).astype(upper.dtype)
        fresh_row = (target - jnp.dot(current, result, precision=highest)) / current[row_index]
        result = jnp.where(positions[:, None] == row_index, fresh_row[None, :], result)
    return result


def factor_pair(moments):
    size = moments.shape[0]
    if size <= 8:
        upper = small_factor(moments)
        return (upper, small_inverse(upper))
    highest = lax.Precision.HIGHEST
    half = size // 2
    upper_one, inverse_one = factor_pair(moments[:half, :half])
    corner = jnp.dot(inverse_one.T, moments[:half, half:], precision=highest)
    rest = moments[half:, half:] - jnp.dot(corner.T, corner, precision=highest)
    upper_two, inverse_two = factor_pair(rest)
    zeros_block = jnp.zeros((size - half, half), moments.dtype)
    upper = jnp.block([[upper_one, corner], [zeros_block, upper_two]])
    inverse_corner = -jnp.dot(
        inverse_one, jnp.dot(corner, inverse_two, precision=highest), precision=highest
    )
    inverse = jnp.block([[inverse_one, inverse_corner], [zeros_block, inverse_two]])
    return (upper, inverse)


def eliminate(augmented_ref, factor_ref, inverse_t_ref):
    matrix = augmented_ref[...]
    size = matrix.shape[0]
    rows = lax.broadcasted_iota(jnp.int32, matrix.shape, 0)
    lanes = lax.broadcasted_iota(jnp.int32, matrix.shape, 1)
    row_ids = rows[:, :1]

    def step(index, matrix):
        pivot_row = jnp.sum(jnp.where(rows == index, matrix, 0.0), axis=0, keepdims=True)
        column = jnp.sum(jnp.where(lanes == index, matrix, 0.0), axis=1, keepdims=True)
        pivot = jnp.sum(jnp.where(lanes[:1] == index, pivot_row, 0.0), axis=1, keepdims=True)
        scale = jnp.where(row_ids > index, column / pivot, 0.0)
        return matrix - scale * pivot_row

    matrix = lax.fori_loop(0, size, step, matrix)
    diagonal = jnp.sum(jnp.where(lanes == rows, matrix, 0.0), axis=1, keepdims=True)
    root = jnp.sqrt(diagonal)
    scaled = matrix / root
    upper = jnp.where(lanes > rows, scaled, jnp.where(lanes == rows, root, 0.0))
    factor_ref[...] = upper[:, :size]
    inverse_t_ref[...] = scaled[:, size:]


def factor_and_inverse_t(gram):
    size = gram.shape[0]
    augmented = jnp.concatenate([gram, jnp.eye(size, dtype=gram.dtype)], axis=1)
    vmem = pl.BlockSpec(memory_space=pltpu.VMEM)
    return pl.pallas_call(
        eliminate,
        out_shape=(
            jax.ShapeDtypeStruct((size, size), gram.dtype),
            jax.ShapeDtypeStruct((size, size), gram.dtype),
        ),
        in_specs=[vmem],
        out_specs=(vmem, vmem),
    )(augmented)


def shards(basis, raw, recur):
    highest = lax.Precision.HIGHEST
    total = basis.shape[0] * lax.axis_size("grp") * lax.axis_size(DEV)
    block = raw - jnp.dot(basis, recur, precision=highest)
    cross, basis_gram, block_gram = packed_total(
        (
            jnp.dot(basis.T, block, precision=highest) / total,
            jnp.dot(basis.T, basis, precision=highest) / total,
            jnp.dot(block.T, block, precision=highest) / total,
        ),
        (DEV, ("grp",)),
    )
    second = cross - jnp.dot(basis_gram, cross, precision=highest)
    coeffs = cross + second
    twice = block - jnp.dot(basis, coeffs, precision=highest)
    mixed = jnp.dot(cross.T, coeffs, precision=highest)
    gram = (
        block_gram
        - mixed
        - mixed.T
        + jnp.dot(coeffs.T, jnp.dot(basis_gram, coeffs, precision=highest), precision=highest)
    )
    gram = 0.5 * (gram + gram.T)
    factor, inverse_t = factor_and_inverse_t(gram)
    lanczos = lax.dot_general(twice, inverse_t, (((1,), (1,)), ((), ())), precision=highest)
    return (lanczos, factor, coeffs)


def solution(mesh):
    torus = Mesh(
        mesh.devices.reshape(mesh.shape["grp"], 4, 4, 2), ("grp", "dev_0", "dev_1", "dev_2")
    )
    in_specs = (P(GRP_DEV, None), P(GRP_DEV, None), P())
    out_specs = (P(GRP_DEV, None), P(), P())
    return jax.shard_map(
        shards, mesh=torus, in_specs=in_specs, out_specs=out_specs, check_vma=False
    )
```
